512 devices in a mesh: tm: 64 (over z, x, y_hi), chan: 8 (over y_lo, core).
Axes of the slice: x: 4, y: 8 (y_hi: 2, y_lo: 4; y = y_hi * 4 + y_lo), z: 8, core: 2. Of those that a mesh axis runs over, the one named last changes fastest.
Arguments:
- field: float32 [2, 2, 64, 65536], P(None, None, 'chan', 'tm'), may hold values from -15.5 to 15.5
- noise: float32 [1, 2, 2, 64, 65536], P(None, None, None, 'chan', 'tm'), may hold values from -1.25 to 1.25
- assign: int32 [64], P('chan'), may hold values from 0 to 63, each once
Outputs:
- received: float32 [2, 2, 64, 65536], P(None, None, 'chan', 'tm')
- recovered: float32 [2, 2, 64, 65536], P(None, None, 'chan', 'tm')
The draws below stay inside these ranges and needn't reach their ends.
All inputs are finite; a program needn't handle non-finite values.
Results may differ from the reference program's by a relative error of at most 0.0003.
Values sent between devices are 32-bit elements; how exact they have to be, the bound alone decides.
No kernel may reach another device: no remote copies, remote signals or barrier semaphores. Data moves between devices by JAX's collectives and lax.ppermute only.
A program may use at most 64 MiB of HBM per device.

```python
import jax
import jax.numpy as jnp
from jax import lax

OPTICAL_CHANNELS = 64
FILTER_HALF_TAPS = 128
STEPS = 2
FIBER_SECTIONS = 1
TIME_SAMPLES = 65536


def draw_field(key, part):
    reference_seed = jax.random.fold_in(key, 0)
    optical_tone_seed = jax.random.fold_in(key, 3)
    shape = (2, 2, OPTICAL_CHANNELS, TIME_SAMPLES)
    ramp = jnp.arange(TIME_SAMPLES, dtype=jnp.int32).astype(jnp.float32) / (TIME_SAMPLES - 1)
    optical_angle_offset = jax.random.uniform(optical_tone_seed, (2, 1, OPTICAL_CHANNELS, 1), jnp.float32, -3.1415927, 3.1415927)
    optical_tone = jnp.concatenate([jnp.cos(optical_angle_offset), jnp.sin(optical_angle_offset)], axis=1)
    reference_signal = jnp.clip(jax.random.normal(reference_seed, shape, jnp.float32), -4.0, 4.0)
    symbol_profile = jnp.sqrt(1.0 + 2.0 * ramp)
    return (0.5 * reference_signal * symbol_profile + 0.4 * optical_tone).astype(jnp.float32)


def draw_noise(key, part):
    rough_key, angle_seed = jax.random.split(key, 2)
    shape = (FIBER_SECTIONS, 2, 2, OPTICAL_CHANNELS, TIME_SAMPLES)
    optical_angle_offset = jax.random.uniform(angle_seed, (FIBER_SECTIONS, 2, 1, OPTICAL_CHANNELS, 1), jnp.float32, -3.1415927, 3.1415927)
    direction_vector = jnp.concatenate([jnp.cos(optical_angle_offset), jnp.sin(optical_angle_offset)], axis=2)
    rough = 0.15 * jnp.clip(jax.random.normal(rough_key, shape, jnp.float32), -6.0, 6.0)
    return (rough + 0.3 * direction_vector).astype(jnp.float32)


def setup_inputs(seed: int = 0) -> dict:
    key_list = jax.random.split(jax.random.key(seed), 4)
    return {
        "field": draw_field(jax.random.fold_in(key_list[3], 71), 0),
        "noise": draw_noise(jax.random.fold_in(key_list[3], 71), 0),
        "assign": jax.random.permutation(key_list[2], OPTICAL_CHANNELS).astype(jnp.int32),
    }


ATT = 0.955
GAMMA = 0.004
WALK = 0.5
SPREAD = 0.4
CHIRP = 0.25
EPS = 1e-06

def tap_tables(channel_ids, sign, reach, channels):
    rows = jnp.arange(3 * reach, dtype=jnp.int32)[:, None]
    cols = jnp.arange(reach, dtype=jnp.int32)[None, :]
    lag = cols - rows + reach
    interior_part = (jnp.abs(lag) <= reach).astype(jnp.float32)
    centre = WALK * reach * (2.0 * channel_ids.astype(jnp.float32) - (channels - 1)) / (channels - 1)
    centre = centre[:, None, None]
    width = SPREAD * reach
    offset = sign * lag.astype(jnp.float32)[None] - centre
    symbol_profile = jnp.exp(-jnp.square(offset / width))
    turn = jnp.square(offset) / (2.0 * CHIRP * reach)
    taps = jnp.arange(-reach, reach + 1, dtype=jnp.int32).astype(jnp.float32)
    scale = jnp.sqrt(lax.optimization_barrier(jnp.sum(jnp.exp(-2.0 * jnp.square((taps[None, :] - centre[:, :, 0]) / width)), axis=1)))
    scale = scale[:, None, None]
    mat_re = interior_part * symbol_profile * jnp.cos(turn) / scale
    mat_im = sign * interior_part * symbol_profile * jnp.sin(turn) / scale
    return (mat_re, mat_im)

def disperse(ext, mat_re, mat_im, reach):
    pols, parts, chans, segment_length = ext.shape
    blocks = segment_length // reach - 2
    rows = ext.reshape(pols, parts, chans, blocks + 2, reach)
    window = jnp.concatenate([rows[:, :, :, 0:blocks], rows[:, :, :, 1:blocks + 1], rows[:, :, :, 2:blocks + 2]], axis=4)
    real = window[:, 0]
    imag = window[:, 1]
    high = lax.Precision.HIGHEST
    out_re = jnp.einsum('pcjq,cqn->pcjn', real, mat_re, precision=high) - jnp.einsum('pcjq,cqn->pcjn', imag, mat_im, precision=high)
    out_im = jnp.einsum('pcjq,cqn->pcjn', real, mat_im, precision=high) + jnp.einsum('pcjq,cqn->pcjn', imag, mat_re, precision=high)
    return jnp.stack([out_re, out_im], axis=1).reshape(pols, parts, chans, blocks * reach)

def rotate(ext, sign, own, total):
    angle = sign * GAMMA * (2.0 * total[None, :] - own)
    cosine = jnp.cos(angle)
    sine = jnp.sin(angle)
    real = ext[:, 0]
    imag = ext[:, 1]
    return jnp.stack([real * cosine - imag * sine, real * sine + imag * cosine], axis=1)

def periodic_filter(current, tables):
    ext = jnp.concatenate([current[..., -FILTER_HALF_TAPS:], current, current[..., :FILTER_HALF_TAPS]], axis=3)

    def single(args):
        piece, m_re, m_im = args
        return disperse(piece[:, :, None], m_re[None], m_im[None], FILTER_HALF_TAPS)[:, :, 0]
    out = lax.map(single, (jnp.moveaxis(ext, 2, 0), tables[0], tables[1]))
    return jnp.moveaxis(out, 0, 2)

def nonlinear(current, sign):
    own = lax.optimization_barrier(jnp.sum(jnp.square(current), axis=(0, 1)))
    total = lax.optimization_barrier(jnp.sum(own, axis=0))
    return rotate(current, sign, own, total)

def slot_power(current):
    return lax.optimization_barrier(jnp.sum(jnp.square(current), axis=(0, 1, 3))) / TIME_SAMPLES

def reference(field, noise, assign):
    forward = tap_tables(assign, 1.0, FILTER_HALF_TAPS, OPTICAL_CHANNELS)
    backward = tap_tables(assign, -1.0, FILTER_HALF_TAPS, OPTICAL_CHANNELS)
    current = field
    for span in range(FIBER_SECTIONS):
        for step in range(STEPS):
            current = periodic_filter(current, forward) * ATT
            current = nonlinear(current, 1.0)
        gain = lax.rsqrt(slot_power(current) + EPS)
        current = current * gain[None, None, :, None] + noise[span]
    received = current
    for span in range(FIBER_SECTIONS):
        rescale = jnp.sqrt(ATT ** (2 * STEPS) / (slot_power(current) + EPS))
        current = current * rescale[None, None, :, None]
        for step in range(STEPS):
            current = nonlinear(current, -1.0) / ATT
            current = periodic_filter(current, backward)
    return (received, current)
```

```python
import jax
import jax.numpy as jnp
from jax import lax
from jax.sharding import Mesh, PartitionSpec as P

OPTICAL_CHANNELS = 64
FILTER_HALF_TAPS = 128
STEPS = 2
FIBER_SECTIONS = 1


ATT = 0.955
GAMMA = 0.004
WALK = 0.5
SPREAD = 0.4
CHIRP = 0.25
EPS = 1e-06


def padded(array, sides, width):
    for axis, dim in sides:
        count, length = (lax.axis_size(axis), array.shape[dim])
        up = [(i, (i + 1) % count) for i in range(count)]
        down = [(j, i) for i, j in up]
        last = lax.slice_in_dim(array, length - width, length, axis=dim)
        leading = lax.slice_in_dim(array, 0, width, axis=dim)
        before = lax.ppermute(last, axis, up)
        after = lax.ppermute(leading, axis, down)
        array = jnp.concatenate([before, array, after], axis=dim)
    return array


def tap_tables(channel_ids, sign, reach, channels):
    rows = jnp.arange(3 * reach, dtype=jnp.int32)[:, None]
    cols = jnp.arange(reach, dtype=jnp.int32)[None, :]
    lag = cols - rows + reach
    interior_part = (jnp.abs(lag) <= reach).astype(jnp.float32)
    centre = (
        WALK * reach * (2.0 * channel_ids.astype(jnp.float32) - (channels - 1)) / (channels - 1)
    )
    centre = centre[:, None, None]
    width = SPREAD * reach
    offset = sign * lag.astype(jnp.float32)[None] - centre
    symbol_profile = jnp.exp(-jnp.square(offset / width))
    turn = jnp.square(offset) / (2.0 * CHIRP * reach)
    taps = jnp.arange(-reach, reach + 1, dtype=jnp.int32).astype(jnp.float32)
    scale = jnp.sqrt(
        jnp.sum(jnp.exp(-2.0 * jnp.square((taps[None, :] - centre[:, :, 0]) / width)), axis=1)
    )
    scale = scale[:, None, None]
    mat_re = interior_part * symbol_profile * jnp.cos(turn) / scale
    mat_im = sign * interior_part * symbol_profile * jnp.sin(turn) / scale
    return (mat_re, mat_im)


def disperse(ext, mat_re, mat_im, reach):
    pols, parts, chans, segment_length = ext.shape
    blocks = segment_length // reach - 2
    rows = ext.reshape(pols, parts, chans, blocks + 2, reach)
    window = jnp.concatenate(
        [rows[:, :, :, 0:blocks], rows[:, :, :, 1 : blocks + 1], rows[:, :, :, 2 : blocks + 2]],
        axis=4,
    )
    real = window[:, 0]
    imag = window[:, 1]
    high = lax.Precision.HIGHEST
    out_re = jnp.einsum("pcjq,cqn->pcjn", real, mat_re, precision=high) - jnp.einsum(
        "pcjq,cqn->pcjn", imag, mat_im, precision=high
    )
    out_im = jnp.einsum("pcjq,cqn->pcjn", real, mat_im, precision=high) + jnp.einsum(
        "pcjq,cqn->pcjn", imag, mat_re, precision=high
    )
    return jnp.stack([out_re, out_im], axis=1).reshape(pols, parts, chans, blocks * reach)


def rotate(ext, sign, own, total):
    angle = sign * GAMMA * (2.0 * total[None, :] - own)
    cosine = jnp.cos(angle)
    sine = jnp.sin(angle)
    real = ext[:, 0]
    imag = ext[:, 1]
    return jnp.stack([real * cosine - imag * sine, real * sine + imag * cosine], axis=1)


TM = ("z", "x", "yh")
CHAN = ("ylo", "core")


def psum_tm(value):
    for axis in ("yh", "x", "z"):
        value = lax.psum(value, axis)
    return value


def psum_chan(value):
    for axis in ("core", "ylo"):
        value = lax.psum(value, axis)
    return value


def on_device(field, noise, assign):
    forward = tap_tables(assign, 1.0, FILTER_HALF_TAPS, OPTICAL_CHANNELS)
    backward = tap_tables(assign, -1.0, FILTER_HALF_TAPS, OPTICAL_CHANNELS)
    total_len = lax.axis_size(TM) * field.shape[3]
    depth = 1
    counts = [min(depth, STEPS - start) for start in range(0, STEPS, depth)]

    def widen(current, count):
        return padded(current, ((TM, 3),), count * FILTER_HALF_TAPS)

    def nonlinear(ext, sign):
        own = jnp.sum(jnp.square(ext), axis=(0, 1))
        total = psum_chan(jnp.sum(own, axis=0))
        return rotate(ext, sign, own, total)

    def channel_power(current):
        summed = psum_tm(jnp.sum(jnp.square(current), axis=(0, 1, 3)))
        return summed / total_len

    current = field
    forward_current = current
    for count in counts:
        ext = widen(forward_current, count)
        ext = disperse(ext, forward[0], forward[1], FILTER_HALF_TAPS) * ATT
        ext = nonlinear(ext, 1.0)
        forward_current = ext
    current = forward_current
    last_noise = noise[FIBER_SECTIONS - 1]
    gain = lax.rsqrt(channel_power(current) + EPS)
    received = current * gain[None, None, :, None] + last_noise
    arrival = channel_power(received)
    current = received
    rescale = jnp.sqrt(ATT ** (2 * STEPS) / (arrival + EPS))
    current = current * rescale[None, None, :, None]
    backward_current = current
    for count in counts:
        ext = widen(backward_current, count)
        ext = nonlinear(ext, -1.0) / ATT
        ext = disperse(ext, backward[0], backward[1], FILTER_HALF_TAPS)
        backward_current = ext
    current = backward_current
    return (received, current)


def solution(mesh):
    tm, chan = mesh.shape["tm"], mesh.shape["chan"]
    fine = Mesh(mesh.devices.reshape(tm // 16, 8, 2, chan // 2, 2), TM + CHAN)
    placed = (P(None, None, CHAN, TM), P(None, None, None, CHAN, TM), P(CHAN))
    return jax.shard_map(
        on_device,
        mesh=fine,
        in_specs=placed,
        out_specs=(P(None, None, CHAN, TM), P(None, None, CHAN, TM)),
        check_vma=False,
    )
```

```python
import jax
import jax.numpy as jnp
from jax import lax
from jax.sharding import Mesh, PartitionSpec as P

OPTICAL_CHANNELS = 64
FILTER_HALF_TAPS = 128
STEPS = 2
FIBER_SECTIONS = 1


ATT = 0.955
GAMMA = 0.004
WALK = 0.5
SPREAD = 0.4
CHIRP = 0.25
EPS = 1e-06


def padded(array, sides, width):
    for axis, dim in sides:
        count, length = (lax.axis_size(axis), array.shape[dim])
        up = [(i, (i + 1) % count) for i in range(count)]
        down = [(j, i) for i, j in up]
        last = lax.slice_in_dim(array, length - width, length, axis=dim)
        leading = lax.slice_in_dim(array, 0, width, axis=dim)
        before = lax.ppermute(last, axis, up)
        after = lax.ppermute(leading, axis, down)
        array = jnp.concatenate([before, array, after], axis=dim)
    return array


def tap_tables(channel_ids, sign, reach, channels):
    rows = jnp.arange(3 * reach, dtype=jnp.int32)[:, None]
    cols = jnp.arange(reach, dtype=jnp.int32)[None, :]
    lag = cols - rows + reach
    interior_part = (jnp.abs(lag) <= reach).astype(jnp.float32)
    centre = (
        WALK * reach * (2.0 * channel_ids.astype(jnp.float32) - (channels - 1)) / (channels - 1)
    )
    centre = centre[:, None, None]
    width = SPREAD * reach
    offset = sign * lag.astype(jnp.float32)[None] - centre
    symbol_profile = jnp.exp(-jnp.square(offset / width))
    turn = jnp.square(offset) / (2.0 * CHIRP * reach)
    taps = jnp.arange(-reach, reach + 1, dtype=jnp.int32).astype(jnp.float32)
    scale = jnp.sqrt(
        jnp.sum(jnp.exp(-2.0 * jnp.square((taps[None, :] - centre[:, :, 0]) / width)), axis=1)
    )
    scale = scale[:, None, None]
    mat_re = interior_part * symbol_profile * jnp.cos(turn) / scale
    mat_im = sign * interior_part * symbol_profile * jnp.sin(turn) / scale
    return (mat_re, mat_im)


def merged_table(mat_re, mat_im):
    top = jnp.concatenate([mat_re, mat_im], axis=2)
    bottom = jnp.concatenate([-mat_im, mat_re], axis=2)
    return jnp.concatenate([top, bottom], axis=1)


def disperse(ext, table, reach):
    pols, parts, chans, segment_length = ext.shape
    blocks = segment_length // reach - 2
    rows = ext.reshape(pols, parts, chans, blocks + 2, reach)
    window = jnp.concatenate(
        [rows[:, :, :, 0:blocks], rows[:, :, :, 1 : blocks + 1], rows[:, :, :, 2 : blocks + 2]],
        axis=4,
    )
    stacked = jnp.moveaxis(window, 1, 3).reshape(pols, chans, blocks, parts * 3 * reach)
    out = jnp.einsum("pcjq,cqn->pcjn", stacked, table, precision=lax.Precision.HIGHEST)
    out = jnp.moveaxis(out.reshape(pols, chans, blocks, parts, reach), 3, 1)
    return out.reshape(pols, parts, chans, blocks * reach)


def rotate(ext, sign, own, total):
    angle = sign * GAMMA * (2.0 * total[None, :] - own)
    cosine = jnp.cos(angle)
    sine = jnp.sin(angle)
    real = ext[:, 0]
    imag = ext[:, 1]
    return jnp.stack([real * cosine - imag * sine, real * sine + imag * cosine], axis=1)


TM = ("z", "x", "yh")
CHAN = ("ylo", "core")


def psum_tm(value):
    for axis in ("yh", "x", "z"):
        value = lax.psum(value, axis)
    return value


def psum_chan(value):
    for axis in ("core", "ylo"):
        value = lax.psum(value, axis)
    return value


def on_device(field, noise, assign):
    forward, backward = lax.optimization_barrier(
        (
            merged_table(*tap_tables(assign, 1.0, FILTER_HALF_TAPS, OPTICAL_CHANNELS)),
            merged_table(*tap_tables(assign, -1.0, FILTER_HALF_TAPS, OPTICAL_CHANNELS)),
        )
    )
    total_len = lax.axis_size(TM) * field.shape[3]
    depth = 1
    counts = [min(depth, STEPS - start) for start in range(0, STEPS, depth)]

    def widen(current, count):
        return padded(current, ((TM, 3),), count * FILTER_HALF_TAPS)

    def nonlinear(ext, sign):
        own = jnp.sum(jnp.square(ext), axis=(0, 1))
        total = psum_chan(jnp.sum(own, axis=0))
        return rotate(ext, sign, own, total)

    def channel_power(current):
        summed = psum_tm(jnp.sum(jnp.square(current), axis=(0, 1, 3)))
        return summed / total_len

    current = field
    forward_current = current
    for count in counts:
        ext = widen(forward_current, count)
        ext = disperse(ext, forward, FILTER_HALF_TAPS) * ATT
        ext = nonlinear(ext, 1.0)
        forward_current = ext
    current = forward_current
    last_noise = noise[FIBER_SECTIONS - 1]
    gain = lax.rsqrt(channel_power(current) + EPS)
    received = current * gain[None, None, :, None] + last_noise
    arrival = channel_power(received)
    current = received
    rescale = jnp.sqrt(ATT ** (2 * STEPS) / (arrival + EPS))
    current = current * rescale[None, None, :, None]
    backward_current = current
    for count in counts:
        ext = widen(backward_current, count)
        ext = nonlinear(ext, -1.0) / ATT
        ext = disperse(ext, backward, FILTER_HALF_TAPS)
        backward_current = ext
    current = backward_current
    return (received, current)


def solution(mesh):
    tm, chan = mesh.shape["tm"], mesh.shape["chan"]
    fine = Mesh(mesh.devices.reshape(tm // 16, 8, 2, chan // 2, 2), TM + CHAN)
    placed = (P(None, None, CHAN, TM), P(None, None, None, CHAN, TM), P(CHAN))
    return jax.shard_map(
        on_device,
        mesh=fine,
        in_specs=placed,
        out_specs=(P(None, None, CHAN, TM), P(None, None, CHAN, TM)),
        check_vma=False,
    )
```

```python
import jax
import jax.numpy as jnp
from jax import lax
from jax.sharding import Mesh, PartitionSpec as P

OPTICAL_CHANNELS = 64
FILTER_HALF_TAPS = 128
STEPS = 2
FIBER_SECTIONS = 1


ATT = 0.955
GAMMA = 0.004
WALK = 0.5
SPREAD = 0.4
CHIRP = 0.25
EPS = 1e-06


def tap_tables(channel_ids, sign, reach, channels):
    rows = jnp.arange(3 * reach, dtype=jnp.int32)[:, None]
    cols = jnp.arange(reach, dtype=jnp.int32)[None, :]
    lag = cols - rows + reach
    interior_part = (jnp.abs(lag) <= reach).astype(jnp.float32)
    centre = (
        WALK * reach * (2.0 * channel_ids.astype(jnp.float32) - (channels - 1)) / (channels - 1)
    )
    centre = centre[:, None, None]
    width = SPREAD * reach
    offset = sign * lag.astype(jnp.float32)[None] - centre
    symbol_profile = jnp.exp(-jnp.square(offset / width))
    turn = jnp.square(offset) / (2.0 * CHIRP * reach)
    taps = jnp.arange(-reach, reach + 1, dtype=jnp.int32).astype(jnp.float32)
    scale = jnp.sqrt(
        jnp.sum(jnp.exp(-2.0 * jnp.square((taps[None, :] - centre[:, :, 0]) / width)), axis=1)
    )
    scale = scale[:, None, None]
    mat_re = interior_part * symbol_profile * jnp.cos(turn) / scale
    mat_im = sign * interior_part * symbol_profile * jnp.sin(turn) / scale
    return (mat_re, mat_im)


def merged_table(mat_re, mat_im):
    top = jnp.concatenate([mat_re, mat_im], axis=2)
    bottom = jnp.concatenate([-mat_im, mat_re], axis=2)
    return jnp.concatenate([top, bottom], axis=1)


def disperse(ext, table, reach):
    pols, parts, chans, segment_length = ext.shape
    blocks = segment_length // reach - 2
    rows = ext.reshape(pols, parts, chans, blocks + 2, reach)
    window = jnp.concatenate(
        [rows[:, :, :, 0:blocks], rows[:, :, :, 1 : blocks + 1], rows[:, :, :, 2 : blocks + 2]],
        axis=4,
    )
    stacked = jnp.moveaxis(window, 1, 3).reshape(pols, chans, blocks, parts * 3 * reach)
    out = jnp.einsum("pcjq,cqn->pcjn", stacked, table, precision=lax.Precision.HIGHEST)
    out = jnp.moveaxis(out.reshape(pols, chans, blocks, parts, reach), 3, 1)
    return out.reshape(pols, parts, chans, blocks * reach)


def rotate(ext, sign, own, total):
    angle = sign * GAMMA * (2.0 * total[None, :] - own)
    cosine = jnp.cos(angle)
    sine = jnp.sin(angle)
    real = ext[:, 0]
    imag = ext[:, 1]
    return jnp.stack([real * cosine - imag * sine, real * sine + imag * cosine], axis=1)


TM = ("z", "x", "yh")
CHAN = ("ylo", "core")


def psum_tm(value):
    for axis in ("yh", "x", "z"):
        value = lax.psum(value, axis)
    return value


def psum_chan(value):
    for axis in ("core", "ylo"):
        value = lax.psum(value, axis)
    return value


def on_device(field, noise, assign):
    forward, backward = lax.optimization_barrier(
        (
            merged_table(*tap_tables(assign, 1.0, FILTER_HALF_TAPS, OPTICAL_CHANNELS)),
            merged_table(*tap_tables(assign, -1.0, FILTER_HALF_TAPS, OPTICAL_CHANNELS)),
        )
    )
    total_len = lax.axis_size(TM) * field.shape[3]
    reach = FILTER_HALF_TAPS
    field_width = 2 * STEPS * reach
    noise_width = STEPS * reach

    def nonlinear(ext, sign):
        own = jnp.sum(jnp.square(ext), axis=(0, 1))
        total = psum_chan(jnp.sum(own, axis=0))
        return rotate(ext, sign, own, total)

    def channel_power(current):
        summed = psum_tm(jnp.sum(jnp.square(current), axis=(0, 1, 3)))
        return summed / total_len

    last_noise = noise[FIBER_SECTIONS - 1]
    count, length = lax.axis_size(TM), field.shape[3]
    up = [(i, (i + 1) % count) for i in range(count)]
    down = [(j, i) for i, j in up]
    trailing = jnp.concatenate(
        [field[..., length - field_width :], last_noise[..., length - noise_width :]], axis=3
    )
    leading = jnp.concatenate([field[..., :field_width], last_noise[..., :noise_width]], axis=3)
    before = lax.ppermute(trailing, TM, up)
    after = lax.ppermute(leading, TM, down)
    current = jnp.concatenate([before[..., :field_width], field, after[..., :field_width]], axis=3)
    noise_ext = jnp.concatenate([before[..., field_width:], last_noise, after[..., field_width:]], axis=3)

    for step in range(STEPS):
        current = disperse(current, forward, reach) * ATT
        current = nonlinear(current, 1.0)
    centre = slice(noise_width, noise_width + length)
    gain = lax.rsqrt(channel_power(current[..., centre]) + EPS)
    current = current * gain[None, None, :, None] + noise_ext
    received = current[..., centre]
    arrival = channel_power(received)
    rescale = jnp.sqrt(ATT ** (2 * STEPS) / (arrival + EPS))
    current = current * rescale[None, None, :, None]
    for step in range(STEPS):
        current = nonlinear(current, -1.0) / ATT
        current = disperse(current, backward, reach)
    return (received, current)


def solution(mesh):
    tm, chan = mesh.shape["tm"], mesh.shape["chan"]
    fine = Mesh(mesh.devices.reshape(tm // 16, 8, 2, chan // 2, 2), TM + CHAN)
    placed = (P(None, None, CHAN, TM), P(None, None, None, CHAN, TM), P(CHAN))
    return jax.shard_map(
        on_device,
        mesh=fine,
        in_specs=placed,
        out_specs=(P(None, None, CHAN, TM), P(None, None, CHAN, TM)),
        check_vma=False,
    )
```

```python
import jax
import jax.numpy as jnp
from jax import lax
from jax.sharding import Mesh, PartitionSpec as P

OPTICAL_CHANNELS = 64
FILTER_HALF_TAPS = 128
STEPS = 2
FIBER_SECTIONS = 1


ATT = 0.955
GAMMA = 0.004
WALK = 0.5
SPREAD = 0.4
CHIRP = 0.25
EPS = 1e-06


def tap_tables(channel_ids, sign, reach, channels):
    rows = jnp.arange(3 * reach, dtype=jnp.int32)[:, None]
    cols = jnp.arange(reach, dtype=jnp.int32)[None, :]
    lag = cols - rows + reach
    interior_part = (jnp.abs(lag) <= reach).astype(jnp.float32)
    centre = (
        WALK * reach * (2.0 * channel_ids.astype(jnp.float32) - (channels - 1)) / (channels - 1)
    )
    centre = centre[:, None, None]
    width = SPREAD * reach
    offset = sign * lag.astype(jnp.float32)[None] - centre
    symbol_profile = jnp.exp(-jnp.square(offset / width))
    turn = jnp.square(offset) / (2.0 * CHIRP * reach)
    taps = jnp.arange(-reach, reach + 1, dtype=jnp.int32).astype(jnp.float32)
    scale = jnp.sqrt(
        jnp.sum(jnp.exp(-2.0 * jnp.square((taps[None, :] - centre[:, :, 0]) / width)), axis=1)
    )
    scale = scale[:, None, None]
    mat_re = interior_part * symbol_profile * jnp.cos(turn) / scale
    mat_im = sign * interior_part * symbol_profile * jnp.sin(turn) / scale
    return (mat_re, mat_im)


def merged_table(mat_re, mat_im):
    top = jnp.concatenate([mat_re, mat_im], axis=2)
    bottom = jnp.concatenate([-mat_im, mat_re], axis=2)
    return jnp.concatenate([top, bottom], axis=1)


def disperse(ext, table, reach):
    pols, parts, chans, segment_length = ext.shape
    blocks = segment_length // reach - 2
    rows = ext.reshape(pols, parts, chans, blocks + 2, reach)
    window = jnp.concatenate(
        [rows[:, :, :, 0:blocks], rows[:, :, :, 1 : blocks + 1], rows[:, :, :, 2 : blocks + 2]],
        axis=4,
    )
    stacked = jnp.moveaxis(window, 1, 3).reshape(pols, chans, blocks, parts * 3 * reach)
    out = jnp.einsum("pcjq,cqn->pcjn", stacked, table, precision=lax.Precision.HIGHEST)
    out = jnp.moveaxis(out.reshape(pols, chans, blocks, parts, reach), 3, 1)
    return out.reshape(pols, parts, chans, blocks * reach)


def rotate(ext, sign, own, total):
    angle = sign * GAMMA * (2.0 * total[None, :] - own)
    cosine = jnp.cos(angle)
    sine = jnp.sin(angle)
    real = ext[:, 0]
    imag = ext[:, 1]
    return jnp.stack([real * cosine - imag * sine, real * sine + imag * cosine], axis=1)


TM = ("z", "x", "yh")
CHAN = ("ylo", "core")


def psum_tm(value):
    for axis in ("yh", "x", "z"):
        value = lax.psum(value, axis)
    return value


def psum_chan(value):
    for axis in ("core", "ylo"):
        value = lax.psum(value, axis)
    return value


def on_device(field, noise, assign):
    forward, backward = lax.optimization_barrier(
        (
            merged_table(*tap_tables(assign, 1.0, FILTER_HALF_TAPS, OPTICAL_CHANNELS)),
            merged_table(*tap_tables(assign, -1.0, FILTER_HALF_TAPS, OPTICAL_CHANNELS)),
        )
    )
    total_len = lax.axis_size(TM) * field.shape[3]
    reach = FILTER_HALF_TAPS
    field_width = 2 * STEPS * reach
    noise_width = STEPS * reach

    def nonlinear(ext, sign):
        own = jnp.sum(jnp.square(ext), axis=(0, 1))
        total = psum_chan(jnp.sum(own, axis=0))
        return rotate(ext, sign, own, total)

    last_noise = noise[FIBER_SECTIONS - 1]
    count, length = lax.axis_size(TM), field.shape[3]
    up = [(i, (i + 1) % count) for i in range(count)]
    down = [(j, i) for i, j in up]
    trailing = jnp.concatenate(
        [field[..., length - field_width :], last_noise[..., length - noise_width :]], axis=3
    )
    leading = jnp.concatenate([field[..., :field_width], last_noise[..., :noise_width]], axis=3)
    before = lax.ppermute(trailing, TM, up)
    after = lax.ppermute(leading, TM, down)
    current = jnp.concatenate([before[..., :field_width], field, after[..., :field_width]], axis=3)
    noise_ext = jnp.concatenate([before[..., field_width:], last_noise, after[..., field_width:]], axis=3)

    for step in range(STEPS):
        current = disperse(current, forward, reach) * ATT
        current = nonlinear(current, 1.0)
    centre = slice(noise_width, noise_width + length)
    signal, added = current[..., centre], last_noise
    sums = psum_tm(
        jnp.stack(
            [
                jnp.sum(jnp.square(signal), axis=(0, 1, 3)),
                jnp.sum(signal * added, axis=(0, 1, 3)),
                jnp.sum(jnp.square(added), axis=(0, 1, 3)),
            ]
        )
    )
    gain = lax.rsqrt(sums[0] / total_len + EPS)
    arrival = (gain * gain * sums[0] + 2.0 * gain * sums[1] + sums[2]) / total_len
    current = current * gain[None, None, :, None] + noise_ext
    received = current[..., centre]
    rescale = jnp.sqrt(ATT ** (2 * STEPS) / (arrival + EPS))
    current = current * rescale[None, None, :, None]
    for step in range(STEPS):
        current = nonlinear(current, -1.0) / ATT
        current = disperse(current, backward, reach)
    return (received, current)


def solution(mesh):
    tm, chan = mesh.shape["tm"], mesh.shape["chan"]
    fine = Mesh(mesh.devices.reshape(tm // 16, 8, 2, chan // 2, 2), TM + CHAN)
    placed = (P(None, None, CHAN, TM), P(None, None, None, CHAN, TM), P(CHAN))
    return jax.shard_map(
        on_device,
        mesh=fine,
        in_specs=placed,
        out_specs=(P(None, None, CHAN, TM), P(None, None, CHAN, TM)),
        check_vma=False,
    )
```

```python
import jax
import jax.numpy as jnp
from jax import lax
from jax.experimental import pallas as pl
from jax.experimental.pallas import tpu as pltpu
from jax.sharding import Mesh, PartitionSpec as P

OPTICAL_CHANNELS = 64
FILTER_HALF_TAPS = 128
STEPS = 2
FIBER_SECTIONS = 1


ATT = 0.955
GAMMA = 0.004
WALK = 0.5
SPREAD = 0.4
CHIRP = 0.25
EPS = 1e-06


def tap_rows(channel_ids, sign, reach, channels):
    lag = jnp.arange(-reach, reach + 1, dtype=jnp.int32).astype(jnp.float32)[None, :]
    centre = WALK * reach * (2.0 * channel_ids.astype(jnp.float32) - (channels - 1)) / (channels - 1)
    centre = centre[:, None]
    width = SPREAD * reach
    offset = sign * lag - centre
    symbol_profile = jnp.exp(-jnp.square(offset / width))
    turn = jnp.square(offset) / (2.0 * CHIRP * reach)
    scale = jnp.sqrt(jnp.sum(jnp.exp(-2.0 * jnp.square((lag - centre) / width)), axis=1))[:, None]
    tap_re = symbol_profile * jnp.cos(turn) / scale
    tap_im = sign * symbol_profile * jnp.sin(turn) / scale
    return jnp.stack([tap_re, tap_im], axis=1)


def toeplitz_kernel(taps_ref, forward_ref, backward_ref):
    for sign, out_ref in enumerate((forward_ref, backward_ref)):
        toeplitz_fill(taps_ref.at[sign], out_ref)


def toeplitz_fill(taps_ref, out_ref):
    reach = out_ref.shape[1] // 2
    for block in range(3):
        start = reach * (2 - block)
        parts = []
        for part in range(2):
            row = taps_ref[part : part + 1, start : start + 2 * reach]
            rolled = pltpu.roll(jnp.broadcast_to(row, (reach, 2 * reach)), 0, 1, stride=1, stride_axis=0)
            parts.append(rolled[:, reach:])
        real, imag = parts
        rows = slice(block * reach, (block + 1) * reach)
        low = slice(3 * reach + block * reach, 3 * reach + (block + 1) * reach)
        out_ref[rows, :reach] = real
        out_ref[rows, reach:] = imag
        out_ref[low, :reach] = -imag
        out_ref[low, reach:] = real


def merged_tables(channel_ids, reach, channels):
    taps = jnp.stack([tap_rows(channel_ids, 1.0, reach, channels), tap_rows(channel_ids, -1.0, reach, channels)], axis=1)
    padded = jnp.pad(taps, ((0, 0), (0, 0), (0, 0), (reach, reach - 1)))
    count = taps.shape[0]
    table = jax.ShapeDtypeStruct((count, 6 * reach, 2 * reach), jnp.float32)
    block = pl.BlockSpec((None, 6 * reach, 2 * reach), lambda s: (s, 0, 0))
    return pl.pallas_call(
        toeplitz_kernel,
        grid=(count,),
        in_specs=[pl.BlockSpec((None, 2, 2, 4 * reach), lambda s: (s, 0, 0, 0))],
        out_specs=(block, block),
        out_shape=(table, table),
    )(padded)


def disperse(ext, table, reach):
    pols, parts, chans, segment_length = ext.shape
    blocks = segment_length // reach - 2
    rows = ext.reshape(pols, parts, chans, blocks + 2, reach)
    window = jnp.concatenate(
        [rows[:, :, :, 0:blocks], rows[:, :, :, 1 : blocks + 1], rows[:, :, :, 2 : blocks + 2]],
        axis=4,
    )
    stacked = jnp.moveaxis(window, 1, 3).reshape(pols, chans, blocks, parts * 3 * reach)
    out = jnp.einsum("pcjq,cqn->pcjn", stacked, table, precision=lax.Precision.HIGHEST)
    out = jnp.moveaxis(out.reshape(pols, chans, blocks, parts, reach), 3, 1)
    return out.reshape(pols, parts, chans, blocks * reach)


def rotate(ext, sign, own, total):
    angle = sign * GAMMA * (2.0 * total[None, :] - own)
    cosine = jnp.cos(angle)
    sine = jnp.sin(angle)
    real = ext[:, 0]
    imag = ext[:, 1]
    return jnp.stack([real * cosine - imag * sine, real * sine + imag * cosine], axis=1)


TM = ("z", "x", "yh")
CHAN = ("ylo", "core")


def psum_tm(value):
    for axis in ("yh", "x", "z"):
        value = lax.psum(value, axis)
    return value


def psum_chan(value):
    for axis in ("core", "ylo"):
        value = lax.psum(value, axis)
    return value


def on_device(field, noise, assign):
    forward, backward = merged_tables(assign, FILTER_HALF_TAPS, OPTICAL_CHANNELS)
    total_len = lax.axis_size(TM) * field.shape[3]
    reach = FILTER_HALF_TAPS
    field_width = 2 * STEPS * reach
    noise_width = STEPS * reach

    def nonlinear(ext, sign):
        own = jnp.sum(jnp.square(ext), axis=(0, 1))
        total = psum_chan(jnp.sum(own, axis=0))
        return rotate(ext, sign, own, total)

    last_noise = noise[FIBER_SECTIONS - 1]
    count, length = lax.axis_size(TM), field.shape[3]
    up = [(i, (i + 1) % count) for i in range(count)]
    down = [(j, i) for i, j in up]
    trailing = jnp.concatenate(
        [field[..., length - field_width :], last_noise[..., length - noise_width :]], axis=3
    )
    leading = jnp.concatenate([field[..., :field_width], last_noise[..., :noise_width]], axis=3)
    before = lax.ppermute(trailing, TM, up)
    after = lax.ppermute(leading, TM, down)
    current = jnp.concatenate([before[..., :field_width], field, after[..., :field_width]], axis=3)
    noise_ext = jnp.concatenate([before[..., field_width:], last_noise, after[..., field_width:]], axis=3)

    for step in range(STEPS):
        current = disperse(current, forward, reach) * ATT
        current = nonlinear(current, 1.0)
    centre = slice(noise_width, noise_width + length)
    signal, added = current[..., centre], last_noise
    sums = psum_tm(
        jnp.stack(
            [
                jnp.sum(jnp.square(signal), axis=(0, 1, 3)),
                jnp.sum(signal * added, axis=(0, 1, 3)),
                jnp.sum(jnp.square(added), axis=(0, 1, 3)),
            ]
        )
    )
    gain = lax.rsqrt(sums[0] / total_len + EPS)
    arrival = (gain * gain * sums[0] + 2.0 * gain * sums[1] + sums[2]) / total_len
    current = current * gain[None, None, :, None] + noise_ext
    received = current[..., centre]
    rescale = jnp.sqrt(ATT ** (2 * STEPS) / (arrival + EPS))
    current = current * rescale[None, None, :, None]
    for step in range(STEPS):
        current = nonlinear(current, -1.0) / ATT
        current = disperse(current, backward, reach)
    return (received, current)


def solution(mesh):
    tm, chan = mesh.shape["tm"], mesh.shape["chan"]
    fine = Mesh(mesh.devices.reshape(tm // 16, 8, 2, chan // 2, 2), TM + CHAN)
    placed = (P(None, None, CHAN, TM), P(None, None, None, CHAN, TM), P(CHAN))
    return jax.shard_map(
        on_device,
        mesh=fine,
        in_specs=placed,
        out_specs=(P(None, None, CHAN, TM), P(None, None, CHAN, TM)),
        check_vma=False,
    )
```

```python
import jax
import jax.numpy as jnp
from jax import lax
from jax.experimental import pallas as pl
from jax.experimental.pallas import tpu as pltpu
from jax.sharding import Mesh, PartitionSpec as P

OPTICAL_CHANNELS = 64
FILTER_HALF_TAPS = 128
STEPS = 2
FIBER_SECTIONS = 1


ATT = 0.955
GAMMA = 0.004
WALK = 0.5
SPREAD = 0.4
CHIRP = 0.25
EPS = 1e-06


def tap_rows(channel_ids, sign, reach, channels):
    lag = jnp.arange(-reach, reach + 1, dtype=jnp.int32).astype(jnp.float32)[None, :]
    centre = WALK * reach * (2.0 * channel_ids.astype(jnp.float32) - (channels - 1)) / (channels - 1)
    centre = centre[:, None]
    width = SPREAD * reach
    offset = sign * lag - centre
    symbol_profile = jnp.exp(-jnp.square(offset / width))
    turn = jnp.square(offset) / (2.0 * CHIRP * reach)
    scale = jnp.sqrt(jnp.sum(jnp.exp(-2.0 * jnp.square((lag - centre) / width)), axis=1))[:, None]
    tap_re = symbol_profile * jnp.cos(turn) / scale
    tap_im = sign * symbol_profile * jnp.sin(turn) / scale
    return jnp.stack([tap_re, tap_im], axis=1)


def toeplitz_kernel(taps_ref, forward_ref, backward_ref):
    for sign, out_ref in enumerate((forward_ref, backward_ref)):
        toeplitz_fill(taps_ref.at[sign], out_ref)


def toeplitz_fill(taps_ref, out_ref):
    reach = out_ref.shape[1] // 2
    for block in range(3):
        start = reach * (2 - block)
        parts = []
        for part in range(2):
            row = taps_ref[part : part + 1, start : start + 2 * reach]
            rolled = pltpu.roll(jnp.broadcast_to(row, (reach, 2 * reach)), 0, 1, stride=1, stride_axis=0)
            parts.append(rolled[:, reach:])
        real, imag = parts
        rows = slice(block * reach, (block + 1) * reach)
        low = slice(3 * reach + block * reach, 3 * reach + (block + 1) * reach)
        out_ref[rows, :reach] = real
        out_ref[rows, reach:] = imag
        out_ref[low, :reach] = -imag
        out_ref[low, reach:] = real


def merged_tables(channel_ids, reach, channels):
    taps = jnp.stack([tap_rows(channel_ids, 1.0, reach, channels), tap_rows(channel_ids, -1.0, reach, channels)], axis=1)
    padded = jnp.pad(taps, ((0, 0), (0, 0), (0, 0), (reach, reach - 1)))
    count = taps.shape[0]
    table = jax.ShapeDtypeStruct((count, 6 * reach, 2 * reach), jnp.float32)
    block = pl.BlockSpec((None, 6 * reach, 2 * reach), lambda s: (s, 0, 0))
    return pl.pallas_call(
        toeplitz_kernel,
        grid=(count,),
        in_specs=[pl.BlockSpec((None, 2, 2, 4 * reach), lambda s: (s, 0, 0, 0))],
        out_specs=(block, block),
        out_shape=(table, table),
    )(padded)


def disperse(ext, table, reach):
    pols, parts, chans, segment_length = ext.shape
    blocks = segment_length // reach - 2
    rows = ext.reshape(pols, parts, chans, blocks + 2, reach)
    window = jnp.concatenate(
        [rows[:, :, :, 0:blocks], rows[:, :, :, 1 : blocks + 1], rows[:, :, :, 2 : blocks + 2]],
        axis=4,
    )
    stacked = jnp.moveaxis(window, 1, 3).reshape(pols, chans, blocks, parts * 3 * reach)
    out = jnp.einsum("pcjq,cqn->pcjn", stacked, table, precision=lax.Precision.HIGHEST)
    out = jnp.moveaxis(out.reshape(pols, chans, blocks, parts, reach), 3, 1)
    return out.reshape(pols, parts, chans, blocks * reach)


def rotate(ext, sign, own, total):
    angle = sign * GAMMA * (2.0 * total[None, :] - own)
    cosine = jnp.cos(angle)
    sine = jnp.sin(angle)
    real = ext[:, 0]
    imag = ext[:, 1]
    return jnp.stack([real * cosine - imag * sine, real * sine + imag * cosine], axis=1)


TM = ("z", "xh", "xl", "yh")
CHAN = ("ylo", "core")


def psum_tm(value):
    for axis in ("yh", "xl", "xh", "z"):
        value = lax.psum(value, axis)
    return value


def psum_chan(value):
    for axis in ("core", "ylo"):
        value = lax.psum(value, axis)
    return value


def on_device(field, noise, assign):
    forward, backward = merged_tables(assign, FILTER_HALF_TAPS, OPTICAL_CHANNELS)
    total_len = lax.axis_size(TM) * field.shape[3]
    reach = FILTER_HALF_TAPS
    field_width = 2 * STEPS * reach
    noise_width = STEPS * reach

    def nonlinear(ext, sign):
        own = jnp.sum(jnp.square(ext), axis=(0, 1))
        total = psum_chan(jnp.sum(own, axis=0))
        return rotate(ext, sign, own, total)

    last_noise = noise[FIBER_SECTIONS - 1]
    count, length = lax.axis_size(TM), field.shape[3]
    up = [(i, (i + 1) % count) for i in range(count)]
    down = [(j, i) for i, j in up]
    trailing = jnp.concatenate(
        [field[..., length - field_width :], last_noise[..., length - noise_width :]], axis=3
    )
    leading = jnp.concatenate([field[..., :field_width], last_noise[..., :noise_width]], axis=3)
    before = lax.ppermute(trailing, TM, up)
    after = lax.ppermute(leading, TM, down)
    current = jnp.concatenate([before[..., :field_width], field, after[..., :field_width]], axis=3)
    noise_ext = jnp.concatenate([before[..., field_width:], last_noise, after[..., field_width:]], axis=3)

    for step in range(STEPS):
        current = disperse(current, forward, reach) * ATT
        current = nonlinear(current, 1.0)
    centre = slice(noise_width, noise_width + length)
    signal, added = current[..., centre], last_noise
    sums = psum_tm(
        jnp.stack(
            [
                jnp.sum(jnp.square(signal), axis=(0, 1, 3)),
                jnp.sum(signal * added, axis=(0, 1, 3)),
                jnp.sum(jnp.square(added), axis=(0, 1, 3)),
            ]
        )
    )
    gain = lax.rsqrt(sums[0] / total_len + EPS)
    arrival = (gain * gain * sums[0] + 2.0 * gain * sums[1] + sums[2]) / total_len
    current = current * gain[None, None, :, None] + noise_ext
    received = current[..., centre]
    rescale = jnp.sqrt(ATT ** (2 * STEPS) / (arrival + EPS))
    current = current * rescale[None, None, :, None]
    for step in range(STEPS):
        current = nonlinear(current, -1.0) / ATT
        current = disperse(current, backward, reach)
    return (received, current)


def solution(mesh):
    tm, chan = mesh.shape["tm"], mesh.shape["chan"]
    fine = Mesh(mesh.devices.reshape(tm // 16, 2, 4, 2, chan // 2, 2), TM + CHAN)
    placed = (P(None, None, CHAN, TM), P(None, None, None, CHAN, TM), P(CHAN))
    return jax.shard_map(
        on_device,
        mesh=fine,
        in_specs=placed,
        out_specs=(P(None, None, CHAN, TM), P(None, None, CHAN, TM)),
        check_vma=False,
    )
```

```python
import jax
import jax.numpy as jnp
from jax import lax
from jax.experimental import pallas as pl
from jax.experimental.pallas import tpu as pltpu
from jax.sharding import Mesh, PartitionSpec as P

OPTICAL_CHANNELS = 64
FILTER_HALF_TAPS = 128
STEPS = 2
FIBER_SECTIONS = 1


ATT = 0.955
GAMMA = 0.004
WALK = 0.5
SPREAD = 0.4
CHIRP = 0.25
EPS = 1e-06


def tap_rows(channel_ids, sign, reach, channels):
    lag = jnp.arange(-reach, reach + 1, dtype=jnp.int32).astype(jnp.float32)[None, :]
    centre = WALK * reach * (2.0 * channel_ids.astype(jnp.float32) - (channels - 1)) / (channels - 1)
    centre = centre[:, None]
    width = SPREAD * reach
    offset = sign * lag - centre
    symbol_profile = jnp.exp(-jnp.square(offset / width))
    turn = jnp.square(offset) / (2.0 * CHIRP * reach)
    scale = jnp.sqrt(jnp.sum(jnp.exp(-2.0 * jnp.square((lag - centre) / width)), axis=1))[:, None]
    tap_re = symbol_profile * jnp.cos(turn) / scale
    tap_im = sign * symbol_profile * jnp.sin(turn) / scale
    return jnp.stack([tap_re, tap_im], axis=1)


def toeplitz_kernel(taps_ref, forward_ref, backward_ref):
    for sign, out_ref in enumerate((forward_ref, backward_ref)):
        toeplitz_fill(taps_ref.at[sign], out_ref)


def toeplitz_fill(taps_ref, out_ref):
    reach = out_ref.shape[1] // 2
    for block in range(3):
        start = reach * (2 - block)
        parts = []
        for part in range(2):
            row = taps_ref[part : part + 1, start : start + 2 * reach]
            rolled = pltpu.roll(jnp.broadcast_to(row, (reach, 2 * reach)), 0, 1, stride=1, stride_axis=0)
            parts.append(rolled[:, reach:])
        real, imag = parts
        rows = slice(block * reach, (block + 1) * reach)
        low = slice(3 * reach + block * reach, 3 * reach + (block + 1) * reach)
        out_ref[rows, :reach] = real
        out_ref[rows, reach:] = imag
        out_ref[low, :reach] = -imag
        out_ref[low, reach:] = real


def merged_tables(channel_ids, reach, channels):
    taps = jnp.stack([tap_rows(channel_ids, 1.0, reach, channels), tap_rows(channel_ids, -1.0, reach, channels)], axis=1)
    padded = jnp.pad(taps, ((0, 0), (0, 0), (0, 0), (reach, reach - 1)))
    count = taps.shape[0]
    table = jax.ShapeDtypeStruct((count, 6 * reach, 2 * reach), jnp.float32)
    block = pl.BlockSpec((None, 6 * reach, 2 * reach), lambda s: (s, 0, 0))
    return pl.pallas_call(
        toeplitz_kernel,
        grid=(count,),
        in_specs=[pl.BlockSpec((None, 2, 2, 4 * reach), lambda s: (s, 0, 0, 0))],
        out_specs=(block, block),
        out_shape=(table, table),
    )(padded)


def disperse(ext, table, reach):
    pols, parts, chans, segment_length = ext.shape
    blocks = segment_length // reach - 2
    rows = ext.reshape(pols, parts, chans, blocks + 2, reach)
    window = jnp.concatenate(
        [rows[:, :, :, 0:blocks], rows[:, :, :, 1 : blocks + 1], rows[:, :, :, 2 : blocks + 2]],
        axis=4,
    )
    stacked = jnp.moveaxis(window, 1, 3).reshape(pols, chans, blocks, parts * 3 * reach)
    out = jnp.einsum("pcjq,cqn->pcjn", stacked, table, precision=lax.Precision.HIGHEST)
    out = jnp.moveaxis(out.reshape(pols, chans, blocks, parts, reach), 3, 1)
    return out.reshape(pols, parts, chans, blocks * reach)


def rotate(ext, sign, own, total):
    angle = sign * GAMMA * (2.0 * total[None, :] - own)
    cosine = jnp.cos(angle)
    sine = jnp.sin(angle)
    real = ext[:, 0]
    imag = ext[:, 1]
    return jnp.stack([real * cosine - imag * sine, real * sine + imag * cosine], axis=1)


TM = ("z", "xh", "xl", "yh")
CHAN = ("ylo", "core")


def psum_tm(value):
    for axis in ("yh", "xl", "xh", "z"):
        value = lax.psum(value, axis)
    return value


def psum_chan(value):
    for axis in ("core", "ylo"):
        value = lax.psum(value, axis)
    return value


def on_device(field, noise, assign):
    forward, backward = merged_tables(assign, FILTER_HALF_TAPS, OPTICAL_CHANNELS)
    total_len = lax.axis_size(TM) * field.shape[3]
    reach = FILTER_HALF_TAPS
    field_width = 2 * STEPS * reach
    noise_width = STEPS * reach

    def nonlinear(ext, sign):
        own = jnp.sum(jnp.square(ext), axis=(0, 1))
        total = psum_chan(jnp.sum(own, axis=0))
        return rotate(ext, sign, own, total)

    last_noise = noise[FIBER_SECTIONS - 1]
    count, length = lax.axis_size(TM), field.shape[3]
    up = [(i, (i + 1) % count) for i in range(count)]
    down = [(j, i) for i, j in up]
    trailing = jnp.concatenate(
        [field[..., length - field_width :], last_noise[..., length - noise_width :]], axis=3
    )
    leading = jnp.concatenate([field[..., :field_width], last_noise[..., :noise_width]], axis=3)
    forward, backward, trailing, leading = lax.optimization_barrier((forward, backward, trailing, leading))
    before = lax.ppermute(trailing, TM, up)
    after = lax.ppermute(leading, TM, down)
    current = jnp.concatenate([before[..., :field_width], field, after[..., :field_width]], axis=3)
    noise_ext = jnp.concatenate([before[..., field_width:], last_noise, after[..., field_width:]], axis=3)

    for step in range(STEPS):
        current = disperse(current, forward, reach) * ATT
        current = nonlinear(current, 1.0)
    centre = slice(noise_width, noise_width + length)
    signal, added = current[..., centre], last_noise
    sums = psum_tm(
        jnp.stack(
            [
                jnp.sum(jnp.square(signal), axis=(0, 1, 3)),
                jnp.sum(signal * added, axis=(0, 1, 3)),
                jnp.sum(jnp.square(added), axis=(0, 1, 3)),
            ]
        )
    )
    gain = lax.rsqrt(sums[0] / total_len + EPS)
    arrival = (gain * gain * sums[0] + 2.0 * gain * sums[1] + sums[2]) / total_len
    current = current * gain[None, None, :, None] + noise_ext
    received = current[..., centre]
    rescale = jnp.sqrt(ATT ** (2 * STEPS) / (arrival + EPS))
    current = current * rescale[None, None, :, None]
    for step in range(STEPS):
        current = nonlinear(current, -1.0) / ATT
        current = disperse(current, backward, reach)
    return (received, current)


def solution(mesh):
    tm, chan = mesh.shape["tm"], mesh.shape["chan"]
    fine = Mesh(mesh.devices.reshape(tm // 16, 2, 4, 2, chan // 2, 2), TM + CHAN)
    placed = (P(None, None, CHAN, TM), P(None, None, None, CHAN, TM), P(CHAN))
    return jax.shard_map(
        on_device,
        mesh=fine,
        in_specs=placed,
        out_specs=(P(None, None, CHAN, TM), P(None, None, CHAN, TM)),
        check_vma=False,
    )
```

```python
import jax
import jax.numpy as jnp
from jax import lax
from jax.experimental import pallas as pl
from jax.experimental.pallas import tpu as pltpu
from jax.sharding import Mesh, PartitionSpec as P

OPTICAL_CHANNELS = 64
FILTER_HALF_TAPS = 128
STEPS = 2
FIBER_SECTIONS = 1


ATT = 0.955
GAMMA = 0.004
WALK = 0.5
SPREAD = 0.4
CHIRP = 0.25
EPS = 1e-06


def tap_rows(channel_ids, sign, reach, channels):
    lag = jnp.arange(-reach, reach + 1, dtype=jnp.int32).astype(jnp.float32)[None, :]
    centre = WALK * reach * (2.0 * channel_ids.astype(jnp.float32) - (channels - 1)) / (channels - 1)
    centre = centre[:, None]
    width = SPREAD * reach
    offset = sign * lag - centre
    symbol_profile = jnp.exp(-jnp.square(offset / width))
    turn = jnp.square(offset) / (2.0 * CHIRP * reach)
    scale = jnp.sqrt(jnp.sum(jnp.exp(-2.0 * jnp.square((lag - centre) / width)), axis=1))[:, None]
    tap_re = symbol_profile * jnp.cos(turn) / scale
    tap_im = sign * symbol_profile * jnp.sin(turn) / scale
    return jnp.stack([tap_re, tap_im], axis=1)


def toeplitz_kernel(taps_ref, forward_ref, backward_ref):
    for sign, out_ref in enumerate((forward_ref, backward_ref)):
        toeplitz_fill(taps_ref.at[sign], out_ref)


def toeplitz_fill(taps_ref, out_ref):
    reach = out_ref.shape[1] // 2
    for block in range(3):
        start = reach * (2 - block)
        parts = []
        for part in range(2):
            row = taps_ref[part : part + 1, start : start + 2 * reach]
            rolled = pltpu.roll(jnp.broadcast_to(row, (reach, 2 * reach)), 0, 1, stride=1, stride_axis=0)
            parts.append(rolled[:, reach:])
        real, imag = parts
        rows = slice(block * reach, (block + 1) * reach)
        low = slice(3 * reach + block * reach, 3 * reach + (block + 1) * reach)
        out_ref[rows, :reach] = real
        out_ref[rows, reach:] = imag
        out_ref[low, :reach] = -imag
        out_ref[low, reach:] = real


def merged_tables(channel_ids, reach, channels):
    taps = jnp.stack([tap_rows(channel_ids, 1.0, reach, channels), tap_rows(channel_ids, -1.0, reach, channels)], axis=1)
    padded = jnp.pad(taps, ((0, 0), (0, 0), (0, 0), (reach, reach - 1)))
    count = taps.shape[0]
    table = jax.ShapeDtypeStruct((count, 6 * reach, 2 * reach), jnp.float32)
    block = pl.BlockSpec((None, 6 * reach, 2 * reach), lambda s: (s, 0, 0))
    return pl.pallas_call(
        toeplitz_kernel,
        grid=(count,),
        in_specs=[pl.BlockSpec((None, 2, 2, 4 * reach), lambda s: (s, 0, 0, 0))],
        out_specs=(block, block),
        out_shape=(table, table),
    )(padded)


def disperse(ext, table, reach):
    pols, parts, chans, segment_length = ext.shape
    blocks = segment_length // reach - 2
    rows = ext.reshape(pols, parts, chans, blocks + 2, reach)
    stacked = jnp.concatenate(
        [rows[:, part, :, shift : shift + blocks] for part in range(parts) for shift in range(3)],
        axis=3,
    )
    out = jnp.einsum("pcjq,cqn->pcjn", stacked, table, precision=lax.Precision.HIGHEST)
    out = jnp.moveaxis(out.reshape(pols, chans, blocks, parts, reach), 3, 1)
    return out.reshape(pols, parts, chans, blocks * reach)


def rotate(ext, sign, own, total):
    angle = sign * GAMMA * (2.0 * total[None, :] - own)
    cosine = jnp.cos(angle)
    sine = jnp.sin(angle)
    real = ext[:, 0]
    imag = ext[:, 1]
    return jnp.stack([real * cosine - imag * sine, real * sine + imag * cosine], axis=1)


TM = ("z", "xh", "xl", "yh")
CHAN = ("ylo", "core")


def psum_tm(value):
    for axis in ("yh", "xl", "xh", "z"):
        value = lax.psum(value, axis)
    return value


def psum_chan(value):
    for axis in ("core", "ylo"):
        value = lax.psum(value, axis)
    return value


def on_device(field, noise, assign):
    forward, backward = merged_tables(assign, FILTER_HALF_TAPS, OPTICAL_CHANNELS)
    total_len = lax.axis_size(TM) * field.shape[3]
    reach = FILTER_HALF_TAPS
    field_width = 2 * STEPS * reach
    noise_width = STEPS * reach

    def nonlinear(ext, sign):
        own = jnp.sum(jnp.square(ext), axis=(0, 1))
        total = psum_chan(jnp.sum(own, axis=0))
        return rotate(ext, sign, own, total)

    last_noise = noise[FIBER_SECTIONS - 1]
    count, length = lax.axis_size(TM), field.shape[3]
    up = [(i, (i + 1) % count) for i in range(count)]
    down = [(j, i) for i, j in up]
    trailing = jnp.concatenate(
        [field[..., length - field_width :], last_noise[..., length - noise_width :]], axis=3
    )
    leading = jnp.concatenate([field[..., :field_width], last_noise[..., :noise_width]], axis=3)
    before = lax.ppermute(trailing, TM, up)
    after = lax.ppermute(leading, TM, down)
    current = jnp.concatenate([before[..., :field_width], field, after[..., :field_width]], axis=3)
    noise_ext = jnp.concatenate([before[..., field_width:], last_noise, after[..., field_width:]], axis=3)

    for step in range(STEPS):
        current = disperse(current, forward, reach) * ATT
        current = nonlinear(current, 1.0)
    centre = slice(noise_width, noise_width + length)
    signal, added = current[..., centre], last_noise
    sums = psum_tm(
        jnp.stack(
            [
                jnp.sum(jnp.square(signal), axis=(0, 1, 3)),
                jnp.sum(signal * added, axis=(0, 1, 3)),
                jnp.sum(jnp.square(added), axis=(0, 1, 3)),
            ]
        )
    )
    gain = lax.rsqrt(sums[0] / total_len + EPS)
    arrival = (gain * gain * sums[0] + 2.0 * gain * sums[1] + sums[2]) / total_len
    current = current * gain[None, None, :, None] + noise_ext
    received = current[..., centre]
    rescale = jnp.sqrt(ATT ** (2 * STEPS) / (arrival + EPS))
    current = current * rescale[None, None, :, None]
    for step in range(STEPS):
        current = nonlinear(current, -1.0) / ATT
        current = disperse(current, backward, reach)
    return (received, current)


def solution(mesh):
    tm, chan = mesh.shape["tm"], mesh.shape["chan"]
    fine = Mesh(mesh.devices.reshape(tm // 16, 2, 4, 2, chan // 2, 2), TM + CHAN)
    placed = (P(None, None, CHAN, TM), P(None, None, None, CHAN, TM), P(CHAN))
    return jax.shard_map(
        on_device,
        mesh=fine,
        in_specs=placed,
        out_specs=(P(None, None, CHAN, TM), P(None, None, CHAN, TM)),
        check_vma=False,
    )
```

```python
import jax
import jax.numpy as jnp
from jax import lax
from jax.experimental import pallas as pl
from jax.experimental.pallas import tpu as pltpu
from jax.sharding import Mesh, PartitionSpec as P

OPTICAL_CHANNELS = 64
FILTER_HALF_TAPS = 128
STEPS = 2
FIBER_SECTIONS = 1


ATT = 0.955
GAMMA = 0.004
WALK = 0.5
SPREAD = 0.4
CHIRP = 0.25
EPS = 1e-06


def tap_rows(channel_ids, sign, reach, channels):
    lag = jnp.arange(-reach, reach + 1, dtype=jnp.int32).astype(jnp.float32)[None, :]
    centre = WALK * reach * (2.0 * channel_ids.astype(jnp.float32) - (channels - 1)) / (channels - 1)
    centre = centre[:, None]
    width = SPREAD * reach
    offset = sign * lag - centre
    symbol_profile = jnp.exp(-jnp.square(offset / width))
    turn = jnp.square(offset) / (2.0 * CHIRP * reach)
    scale = jnp.sqrt(jnp.sum(jnp.exp(-2.0 * jnp.square((lag - centre) / width)), axis=1))[:, None]
    tap_re = symbol_profile * jnp.cos(turn) / scale
    tap_im = sign * symbol_profile * jnp.sin(turn) / scale
    return jnp.stack([tap_re, tap_im], axis=1)


def toeplitz_kernel(taps_ref, forward_ref, backward_ref):
    for slot in range(taps_ref.shape[0]):
        for sign, out_ref in enumerate((forward_ref, backward_ref)):
            toeplitz_fill(taps_ref.at[slot, sign], out_ref.at[slot])


def toeplitz_fill(taps_ref, out_ref):
    reach = out_ref.shape[-1] // 2
    for block in range(3):
        start = reach * (2 - block)
        parts = []
        for part in range(2):
            row = taps_ref[part : part + 1, start : start + 2 * reach]
            rolled = pltpu.roll(jnp.broadcast_to(row, (reach, 2 * reach)), 0, 1, stride=1, stride_axis=0)
            parts.append(rolled[:, reach:])
        real, imag = parts
        rows = slice(block * reach, (block + 1) * reach)
        low = slice(3 * reach + block * reach, 3 * reach + (block + 1) * reach)
        out_ref[rows, :reach] = real
        out_ref[rows, reach:] = imag
        out_ref[low, :reach] = -imag
        out_ref[low, reach:] = real


def merged_tables(channel_ids, reach, channels):
    taps = jnp.stack([tap_rows(channel_ids, 1.0, reach, channels), tap_rows(channel_ids, -1.0, reach, channels)], axis=1)
    padded = jnp.pad(taps, ((0, 0), (0, 0), (0, 0), (reach, reach - 1)))
    count = taps.shape[0]
    table = jax.ShapeDtypeStruct((count, 6 * reach, 2 * reach), jnp.float32)
    per = 2
    block = pl.BlockSpec((per, 6 * reach, 2 * reach), lambda s: (s, 0, 0))
    return pl.pallas_call(
        toeplitz_kernel,
        grid=(count // per,),
        in_specs=[pl.BlockSpec((per, 2, 2, 4 * reach), lambda s: (s, 0, 0, 0))],
        out_specs=(block, block),
        out_shape=(table, table),
    )(padded)


def disperse(ext, table, reach):
    pols, parts, chans, segment_length = ext.shape
    blocks = segment_length // reach - 2
    rows = ext.reshape(pols, parts, chans, blocks + 2, reach)
    stacked = jnp.concatenate(
        [rows[:, part, :, shift : shift + blocks] for part in range(parts) for shift in range(3)],
        axis=3,
    )
    out = jnp.einsum("pcjq,cqn->pcjn", stacked, table, precision=lax.Precision.HIGHEST)
    out = jnp.moveaxis(out.reshape(pols, chans, blocks, parts, reach), 3, 1)
    return out.reshape(pols, parts, chans, blocks * reach)


def rotate(ext, sign, own, total):
    angle = sign * GAMMA * (2.0 * total[None, :] - own)
    cosine = jnp.cos(angle)
    sine = jnp.sin(angle)
    real = ext[:, 0]
    imag = ext[:, 1]
    return jnp.stack([real * cosine - imag * sine, real * sine + imag * cosine], axis=1)


TM = ("z", "xh", "xl", "yh")
CHAN = ("ylo", "core")


def psum_tm(value):
    for axis in ("yh", "xl", "xh", "z"):
        value = lax.psum(value, axis)
    return value


def psum_chan(value):
    for axis in ("core", "ylo"):
        value = lax.psum(value, axis)
    return value


def on_device(field, noise, assign):
    forward, backward = merged_tables(assign, FILTER_HALF_TAPS, OPTICAL_CHANNELS)
    total_len = lax.axis_size(TM) * field.shape[3]
    reach = FILTER_HALF_TAPS
    field_width = 2 * STEPS * reach
    noise_width = STEPS * reach

    def nonlinear(ext, sign):
        own = jnp.sum(jnp.square(ext), axis=(0, 1))
        total = psum_chan(jnp.sum(own, axis=0))
        return rotate(ext, sign, own, total)

    last_noise = noise[FIBER_SECTIONS - 1]
    count, length = lax.axis_size(TM), field.shape[3]
    up = [(i, (i + 1) % count) for i in range(count)]
    down = [(j, i) for i, j in up]
    trailing = jnp.concatenate(
        [field[..., length - field_width :], last_noise[..., length - noise_width :]], axis=3
    )
    leading = jnp.concatenate([field[..., :field_width], last_noise[..., :noise_width]], axis=3)
    before = lax.ppermute(trailing, TM, up)
    after = lax.ppermute(leading, TM, down)
    current = jnp.concatenate([before[..., :field_width], field, after[..., :field_width]], axis=3)
    noise_ext = jnp.concatenate([before[..., field_width:], last_noise, after[..., field_width:]], axis=3)

    for step in range(STEPS):
        current = disperse(current, forward, reach) * ATT
        current = nonlinear(current, 1.0)
    centre = slice(noise_width, noise_width + length)
    signal, added = current[..., centre], last_noise
    sums = psum_tm(
        jnp.stack(
            [
                jnp.sum(jnp.square(signal), axis=(0, 1, 3)),
                jnp.sum(signal * added, axis=(0, 1, 3)),
                jnp.sum(jnp.square(added), axis=(0, 1, 3)),
            ]
        )
    )
    gain = lax.rsqrt(sums[0] / total_len + EPS)
    arrival = (gain * gain * sums[0] + 2.0 * gain * sums[1] + sums[2]) / total_len
    current = current * gain[None, None, :, None] + noise_ext
    received = current[..., centre]
    rescale = jnp.sqrt(ATT ** (2 * STEPS) / (arrival + EPS))
    current = current * rescale[None, None, :, None]
    for step in range(STEPS):
        current = nonlinear(current, -1.0) / ATT
        current = disperse(current, backward, reach)
    return (received, current)


def solution(mesh):
    tm, chan = mesh.shape["tm"], mesh.shape["chan"]
    fine = Mesh(mesh.devices.reshape(tm // 16, 2, 4, 2, chan // 2, 2), TM + CHAN)
    placed = (P(None, None, CHAN, TM), P(None, None, None, CHAN, TM), P(CHAN))
    return jax.shard_map(
        on_device,
        mesh=fine,
        in_specs=placed,
        out_specs=(P(None, None, CHAN, TM), P(None, None, CHAN, TM)),
        check_vma=False,
    )
```

```python
import jax
import jax.numpy as jnp
from jax import lax
from jax.experimental import pallas as pl
from jax.experimental.pallas import tpu as pltpu
from jax.sharding import Mesh, PartitionSpec as P

OPTICAL_CHANNELS = 64
FILTER_HALF_TAPS = 128
STEPS = 2
FIBER_SECTIONS = 1


ATT = 0.955
GAMMA = 0.004
WALK = 0.5
SPREAD = 0.4
CHIRP = 0.25
EPS = 1e-06


def tap_rows(channel_ids, sign, reach, channels):
    lag = jnp.arange(-reach, reach + 1, dtype=jnp.int32).astype(jnp.float32)[None, :]
    centre = WALK * reach * (2.0 * channel_ids.astype(jnp.float32) - (channels - 1)) / (channels - 1)
    centre = centre[:, None]
    width = SPREAD * reach
    offset = sign * lag - centre
    symbol_profile = jnp.exp(-jnp.square(offset / width))
    turn = jnp.square(offset) / (2.0 * CHIRP * reach)
    scale = jnp.sqrt(jnp.sum(jnp.exp(-2.0 * jnp.square((lag - centre) / width)), axis=1))[:, None]
    tap_re = symbol_profile * jnp.cos(turn) / scale
    tap_im = sign * symbol_profile * jnp.sin(turn) / scale
    return jnp.stack([tap_re, tap_im], axis=1)


def toeplitz_kernel(taps_ref, forward_ref, backward_ref):
    for slot in range(taps_ref.shape[0]):
        for sign, out_ref in enumerate((forward_ref, backward_ref)):
            toeplitz_fill(taps_ref.at[slot, sign], out_ref.at[slot])


def toeplitz_fill(taps_ref, out_ref):
    reach = out_ref.shape[-1] // 2
    for block in range(3):
        start = reach * (2 - block)
        parts = []
        for part in range(2):
            row = taps_ref[part : part + 1, start : start + 2 * reach]
            rolled = pltpu.roll(jnp.broadcast_to(row, (reach, 2 * reach)), 0, 1, stride=1, stride_axis=0)
            parts.append(rolled[:, reach:])
        real, imag = parts
        rows = slice(block * reach, (block + 1) * reach)
        out_ref[rows, :reach] = real
        out_ref[rows, reach:] = imag


def merged_tables(channel_ids, reach, channels):
    taps = jnp.stack([tap_rows(channel_ids, 1.0, reach, channels), tap_rows(channel_ids, -1.0, reach, channels)], axis=1)
    padded = jnp.pad(taps, ((0, 0), (0, 0), (0, 0), (reach, reach - 1)))
    count = taps.shape[0]
    table = jax.ShapeDtypeStruct((count, 3 * reach, 2 * reach), jnp.float32)
    per = 2
    block = pl.BlockSpec((per, 3 * reach, 2 * reach), lambda s: (s, 0, 0))
    return pl.pallas_call(
        toeplitz_kernel,
        grid=(count // per,),
        in_specs=[pl.BlockSpec((per, 2, 2, 4 * reach), lambda s: (s, 0, 0, 0))],
        out_specs=(block, block),
        out_shape=(table, table),
    )(padded)


def disperse(ext, table, reach):
    pols, parts, chans, segment_length = ext.shape
    blocks = segment_length // reach - 2
    rows = ext.reshape(pols, parts, chans, blocks + 2, reach)
    stacked = jnp.concatenate([rows[:, :, :, shift : shift + blocks] for shift in range(3)], axis=4)
    out = jnp.einsum("pacjq,cqn->pacjn", stacked, table, precision=lax.Precision.HIGHEST)
    from_re, from_im = out[:, 0], out[:, 1]
    real = from_re[..., :reach] - from_im[..., reach:]
    imag = from_re[..., reach:] + from_im[..., :reach]
    return jnp.stack([real, imag], axis=1).reshape(pols, parts, chans, blocks * reach)


def rotate(ext, sign, own, total):
    angle = sign * GAMMA * (2.0 * total[None, :] - own)
    cosine = jnp.cos(angle)
    sine = jnp.sin(angle)
    real = ext[:, 0]
    imag = ext[:, 1]
    return jnp.stack([real * cosine - imag * sine, real * sine + imag * cosine], axis=1)


TM = ("z", "xh", "xl", "yh")
CHAN = ("ylo", "core")


def psum_tm(value):
    for axis in ("yh", "xl", "xh", "z"):
        value = lax.psum(value, axis)
    return value


def psum_chan(value):
    for axis in ("core", "ylo"):
        value = lax.psum(value, axis)
    return value


def on_device(field, noise, assign):
    forward, backward = merged_tables(assign, FILTER_HALF_TAPS, OPTICAL_CHANNELS)
    total_len = lax.axis_size(TM) * field.shape[3]
    reach = FILTER_HALF_TAPS
    field_width = 2 * STEPS * reach
    noise_width = STEPS * reach

    def nonlinear(ext, sign):
        own = jnp.sum(jnp.square(ext), axis=(0, 1))
        total = psum_chan(jnp.sum(own, axis=0))
        return rotate(ext, sign, own, total)

    last_noise = noise[FIBER_SECTIONS - 1]
    count, length = lax.axis_size(TM), field.shape[3]
    up = [(i, (i + 1) % count) for i in range(count)]
    down = [(j, i) for i, j in up]
    trailing = jnp.concatenate(
        [field[..., length - field_width :], last_noise[..., length - noise_width :]], axis=3
    )
    leading = jnp.concatenate([field[..., :field_width], last_noise[..., :noise_width]], axis=3)
    before = lax.ppermute(trailing, TM, up)
    after = lax.ppermute(leading, TM, down)
    current = jnp.concatenate([before[..., :field_width], field, after[..., :field_width]], axis=3)
    noise_ext = jnp.concatenate([before[..., field_width:], last_noise, after[..., field_width:]], axis=3)

    for step in range(STEPS):
        current = disperse(current, forward, reach) * ATT
        current = nonlinear(current, 1.0)
    centre = slice(noise_width, noise_width + length)
    signal, added = current[..., centre], last_noise
    sums = psum_tm(
        jnp.stack(
            [
                jnp.sum(jnp.square(signal), axis=(0, 1, 3)),
                jnp.sum(signal * added, axis=(0, 1, 3)),
                jnp.sum(jnp.square(added), axis=(0, 1, 3)),
            ]
        )
    )
    gain = lax.rsqrt(sums[0] / total_len + EPS)
    arrival = (gain * gain * sums[0] + 2.0 * gain * sums[1] + sums[2]) / total_len
    current = current * gain[None, None, :, None] + noise_ext
    received = current[..., centre]
    rescale = jnp.sqrt(ATT ** (2 * STEPS) / (arrival + EPS))
    current = current * rescale[None, None, :, None]
    for step in range(STEPS):
        current = nonlinear(current, -1.0) / ATT
        current = disperse(current, backward, reach)
    return (received, current)


def solution(mesh):
    tm, chan = mesh.shape["tm"], mesh.shape["chan"]
    fine = Mesh(mesh.devices.reshape(tm // 16, 2, 4, 2, chan // 2, 2), TM + CHAN)
    placed = (P(None, None, CHAN, TM), P(None, None, None, CHAN, TM), P(CHAN))
    return jax.shard_map(
        on_device,
        mesh=fine,
        in_specs=placed,
        out_specs=(P(None, None, CHAN, TM), P(None, None, CHAN, TM)),
        check_vma=False,
    )
```

```python
import jax
import jax.numpy as jnp
from jax import lax
from jax.experimental import pallas as pl
from jax.experimental.pallas import tpu as pltpu
from jax.sharding import Mesh, PartitionSpec as P

OPTICAL_CHANNELS = 64
FILTER_HALF_TAPS = 128
STEPS = 2
FIBER_SECTIONS = 1


ATT = 0.955
GAMMA = 0.004
WALK = 0.5
SPREAD = 0.4
CHIRP = 0.25
EPS = 1e-06


def tap_rows(channel_ids, sign, reach, channels):
    lag = jnp.arange(-reach, reach + 1, dtype=jnp.int32).astype(jnp.float32)[None, :]
    centre = WALK * reach * (2.0 * channel_ids.astype(jnp.float32) - (channels - 1)) / (channels - 1)
    centre = centre[:, None]
    width = SPREAD * reach
    offset = sign * lag - centre
    symbol_profile = jnp.exp(-jnp.square(offset / width))
    turn = jnp.square(offset) / (2.0 * CHIRP * reach)
    scale = jnp.sqrt(jnp.sum(jnp.exp(-2.0 * jnp.square((lag - centre) / width)), axis=1))[:, None]
    tap_re = symbol_profile * jnp.cos(turn) / scale
    tap_im = sign * symbol_profile * jnp.sin(turn) / scale
    return jnp.stack([tap_re, tap_im], axis=1)


def toeplitz_kernel(taps_ref, forward_ref, backward_ref):
    for slot in range(taps_ref.shape[0]):
        for sign, out_ref in enumerate((forward_ref, backward_ref)):
            toeplitz_fill(taps_ref.at[slot, sign], out_ref.at[slot])


def toeplitz_fill(taps_ref, out_ref):
    reach = out_ref.shape[-1] // 2
    for block in range(3):
        start = reach * (2 - block)
        parts = []
        for part in range(2):
            row = taps_ref[part : part + 1, start : start + 2 * reach]
            rolled = pltpu.roll(jnp.broadcast_to(row, (reach, 2 * reach)), 0, 1, stride=1, stride_axis=0)
            parts.append(rolled[:, reach:])
        real, imag = parts
        rows = slice(block * reach, (block + 1) * reach)
        out_ref[rows, :reach] = real
        out_ref[rows, reach:] = imag


def merged_tables(channel_ids, reach, channels):
    taps = jnp.stack([tap_rows(channel_ids, 1.0, reach, channels), tap_rows(channel_ids, -1.0, reach, channels)], axis=1)
    padded = jnp.pad(taps, ((0, 0), (0, 0), (0, 0), (reach, reach - 1)))
    count = taps.shape[0]
    table = jax.ShapeDtypeStruct((count, 3 * reach, 2 * reach), jnp.float32)
    per = 2
    block = pl.BlockSpec((per, 3 * reach, 2 * reach), lambda s: (s, 0, 0))
    return pl.pallas_call(
        toeplitz_kernel,
        grid=(count // per,),
        in_specs=[pl.BlockSpec((per, 2, 2, 4 * reach), lambda s: (s, 0, 0, 0))],
        out_specs=(block, block),
        out_shape=(table, table),
    )(padded)


def disperse(ext, table, reach):
    pols, parts, chans, segment_length = ext.shape
    blocks = segment_length // reach - 2
    rows = ext.reshape(pols, parts, chans, blocks + 2, reach)
    stacked = jnp.concatenate([rows[:, :, :, shift : shift + blocks] for shift in range(3)], axis=4)
    out = jnp.einsum("pacjq,cqn->pacjn", stacked, table, precision=lax.Precision.HIGHEST)
    from_re, from_im = out[:, 0], out[:, 1]
    real = from_re[..., :reach] - from_im[..., reach:]
    imag = from_re[..., reach:] + from_im[..., :reach]
    return jnp.stack([real, imag], axis=1).reshape(pols, parts, chans, blocks * reach)


def rotate(ext, sign, own, total):
    angle = sign * GAMMA * (2.0 * total[None, :] - own)
    cosine = jnp.cos(angle)
    sine = jnp.sin(angle)
    real = ext[:, 0]
    imag = ext[:, 1]
    return jnp.stack([real * cosine - imag * sine, real * sine + imag * cosine], axis=1)


TM = ("z", "xh", "xl", "yh")
CHAN = ("ylo", "core")


def psum_tm(value):
    for axis in ("yh", "xl", "xh", "z"):
        value = lax.psum(value, axis)
    return value


def psum_chan(value):
    for axis in ("core", "ylo"):
        value = lax.psum(value, axis)
    return value


def on_device(field, noise, assign):
    forward, backward = merged_tables(assign, FILTER_HALF_TAPS, OPTICAL_CHANNELS)
    total_len = lax.axis_size(TM) * field.shape[3]
    reach = FILTER_HALF_TAPS
    field_width = 2 * STEPS * reach
    noise_width = STEPS * reach

    def nonlinear(ext, sign):
        own = jnp.sum(jnp.square(ext), axis=(0, 1))
        total = psum_chan(jnp.sum(own, axis=0))
        return rotate(ext, sign, own, total)

    last_noise = noise[FIBER_SECTIONS - 1]
    count, length = lax.axis_size(TM), field.shape[3]
    up = [(i, (i + 1) % count) for i in range(count)]
    down = [(j, i) for i, j in up]
    trailing = jnp.concatenate(
        [field[..., length - field_width :], last_noise[..., length - noise_width :]], axis=3
    )
    leading = jnp.concatenate([field[..., :field_width], last_noise[..., :noise_width]], axis=3)
    before = lax.ppermute(trailing, TM, up)
    after = lax.ppermute(leading, TM, down)
    current = jnp.concatenate([before[..., :field_width], field, after[..., :field_width]], axis=3)
    noise_ext = jnp.concatenate([before[..., field_width:], last_noise, after[..., field_width:]], axis=3)

    for step in range(STEPS):
        current = disperse(current, forward, reach) * ATT
        current = nonlinear(current, 1.0)
    centre = slice(noise_width, noise_width + length)
    signal, added = current[..., centre], last_noise
    sums = psum_tm(
        jnp.stack(
            [
                jnp.sum(jnp.square(signal), axis=(0, 1, 3)),
                jnp.sum(signal * added, axis=(0, 1, 3)),
                jnp.sum(jnp.square(added), axis=(0, 1, 3)),
            ]
        )
    )
    gain = lax.rsqrt(sums[0] / total_len + EPS)
    arrival = (gain * gain * sums[0] + 2.0 * gain * sums[1] + sums[2]) / total_len
    received = signal * gain[None, None, :, None] + added
    current = current * gain[None, None, :, None] + noise_ext
    rescale = jnp.sqrt(ATT ** (2 * STEPS) / (arrival + EPS))
    current = current * rescale[None, None, :, None]
    for step in range(STEPS):
        current = nonlinear(current, -1.0) / ATT
        current = disperse(current, backward, reach)
    return (received, current)


def solution(mesh):
    tm, chan = mesh.shape["tm"], mesh.shape["chan"]
    fine = Mesh(mesh.devices.reshape(tm // 16, 2, 4, 2, chan // 2, 2), TM + CHAN)
    placed = (P(None, None, CHAN, TM), P(None, None, None, CHAN, TM), P(CHAN))
    return jax.shard_map(
        on_device,
        mesh=fine,
        in_specs=placed,
        out_specs=(P(None, None, CHAN, TM), P(None, None, CHAN, TM)),
        check_vma=False,
    )
```

```python
import jax
import jax.numpy as jnp
from jax import lax
from jax.experimental import pallas as pl
from jax.experimental.pallas import tpu as pltpu
from jax.sharding import Mesh, PartitionSpec as P

OPTICAL_CHANNELS = 64
FILTER_HALF_TAPS = 128
STEPS = 2
FIBER_SECTIONS = 1


ATT = 0.955
GAMMA = 0.004
WALK = 0.5
SPREAD = 0.4
CHIRP = 0.25
EPS = 1e-06


def tap_rows(channel_ids, sign, reach, channels):
    lag = jnp.arange(-reach, reach + 1, dtype=jnp.int32).astype(jnp.float32)[None, :]
    centre = WALK * reach * (2.0 * channel_ids.astype(jnp.float32) - (channels - 1)) / (channels - 1)
    centre = centre[:, None]
    width = SPREAD * reach
    offset = sign * lag - centre
    symbol_profile = jnp.exp(-jnp.square(offset / width))
    turn = jnp.square(offset) / (2.0 * CHIRP * reach)
    scale = jnp.sqrt(jnp.sum(jnp.exp(-2.0 * jnp.square((lag - centre) / width)), axis=1))[:, None]
    tap_re = symbol_profile * jnp.cos(turn) / scale
    tap_im = sign * symbol_profile * jnp.sin(turn) / scale
    return jnp.stack([tap_re, tap_im], axis=1)


def toeplitz_kernel(taps_ref, forward_ref, backward_ref):
    for slot in range(taps_ref.shape[0]):
        for sign, out_ref in enumerate((forward_ref, backward_ref)):
            toeplitz_fill(taps_ref.at[slot, sign], out_ref.at[slot])


def toeplitz_fill(taps_ref, out_ref):
    reach = out_ref.shape[-1] // 2
    for block in range(3):
        start = reach * (2 - block)
        parts = []
        for part in range(2):
            row = taps_ref[part : part + 1, start : start + 2 * reach]
            rolled = pltpu.roll(jnp.broadcast_to(row, (reach, 2 * reach)), 0, 1, stride=1, stride_axis=0)
            parts.append(rolled[:, reach:])
        real, imag = parts
        rows = slice(block * reach, (block + 1) * reach)
        out_ref[rows, :reach] = real
        out_ref[rows, reach:] = imag


def merged_tables(channel_ids, reach, channels):
    taps = jnp.stack([tap_rows(channel_ids, 1.0, reach, channels), tap_rows(channel_ids, -1.0, reach, channels)], axis=1)
    padded = jnp.pad(taps, ((0, 0), (0, 0), (0, 0), (reach, reach - 1)))
    count = taps.shape[0]
    table = jax.ShapeDtypeStruct((count, 3 * reach, 2 * reach), jnp.float32)
    per = 2
    block = pl.BlockSpec((per, 3 * reach, 2 * reach), lambda s: (s, 0, 0))
    return pl.pallas_call(
        toeplitz_kernel,
        grid=(count // per,),
        in_specs=[pl.BlockSpec((per, 2, 2, 4 * reach), lambda s: (s, 0, 0, 0))],
        out_specs=(block, block),
        out_shape=(table, table),
    )(padded)


def disperse(ext, table, reach):
    pols, parts, chans, segment_length = ext.shape
    blocks = segment_length // reach - 2
    rows = ext.reshape(pols, parts, chans, blocks + 2, reach)
    stacked = jnp.concatenate([rows[:, :, :, shift : shift + blocks] for shift in range(3)], axis=4)
    out = jnp.einsum("pacjq,cqn->pacjn", stacked, table, precision=lax.Precision.HIGHEST)
    from_re, from_im = out[:, 0], out[:, 1]
    real = from_re[..., :reach] - from_im[..., reach:]
    imag = from_re[..., reach:] + from_im[..., :reach]
    return jnp.stack([real, imag], axis=1).reshape(pols, parts, chans, blocks * reach)


def rotate(ext, sign, own, total):
    angle = sign * GAMMA * (2.0 * total[None, :] - own)
    cosine = jnp.cos(angle)
    sine = jnp.sin(angle)
    real = ext[:, 0]
    imag = ext[:, 1]
    return jnp.stack([real * cosine - imag * sine, real * sine + imag * cosine], axis=1)


TM = ("z", "xh", "xl", "yh")
CHAN = ("ylo", "core")


def psum_tm(value):
    for axis in ("yh", "xl", "xh", "z"):
        value = lax.psum(value, axis)
    return value


def psum_chan(value):
    for axis in ("core", "ylo"):
        value = lax.psum(value, axis)
    return value


def on_device(field, noise, assign):
    forward, backward = merged_tables(assign, FILTER_HALF_TAPS, OPTICAL_CHANNELS)
    total_len = lax.axis_size(TM) * field.shape[3]
    reach = FILTER_HALF_TAPS
    field_width = 2 * STEPS * reach
    noise_width = STEPS * reach

    def nonlinear(ext, sign):
        own = jnp.sum(jnp.square(ext), axis=(0, 1))
        total = psum_chan(jnp.sum(own, axis=0))
        return rotate(ext, sign, own, total)

    last_noise = noise[FIBER_SECTIONS - 1]
    count, length = lax.axis_size(TM), field.shape[3]
    up = [(i, (i + 1) % count) for i in range(count)]
    down = [(j, i) for i, j in up]
    trailing = jnp.concatenate(
        [field[..., length - field_width :], last_noise[..., length - noise_width :]], axis=3
    )
    leading = jnp.concatenate([field[..., :field_width], last_noise[..., :noise_width]], axis=3)
    before = lax.ppermute(trailing, TM, up)
    after = lax.ppermute(leading, TM, down)
    noise_ext = jnp.concatenate([before[..., field_width:], last_noise, after[..., field_width:]], axis=3)

    edge = 2 * reach
    current = jnp.concatenate(
        [
            disperse(jnp.concatenate([before[..., :field_width], field[..., :edge]], axis=3), forward, reach),
            disperse(field, forward, reach),
            disperse(jnp.concatenate([field[..., length - edge :], after[..., :field_width]], axis=3), forward, reach),
        ],
        axis=3,
    )
    for step in range(STEPS):
        if step:
            current = disperse(current, forward, reach)
        current = nonlinear(current * ATT, 1.0)
    centre = slice(noise_width, noise_width + length)
    signal, added = current[..., centre], last_noise
    sums = psum_tm(
        jnp.stack(
            [
                jnp.sum(jnp.square(signal), axis=(0, 1, 3)),
                jnp.sum(signal * added, axis=(0, 1, 3)),
                jnp.sum(jnp.square(added), axis=(0, 1, 3)),
            ]
        )
    )
    gain = lax.rsqrt(sums[0] / total_len + EPS)
    arrival = (gain * gain * sums[0] + 2.0 * gain * sums[1] + sums[2]) / total_len
    received = signal * gain[None, None, :, None] + added
    current = current * gain[None, None, :, None] + noise_ext
    rescale = jnp.sqrt(ATT ** (2 * STEPS) / (arrival + EPS))
    current = current * rescale[None, None, :, None]
    for step in range(STEPS):
        current = nonlinear(current, -1.0) / ATT
        current = disperse(current, backward, reach)
    return (received, current)


def solution(mesh):
    tm, chan = mesh.shape["tm"], mesh.shape["chan"]
    fine = Mesh(mesh.devices.reshape(tm // 16, 2, 4, 2, chan // 2, 2), TM + CHAN)
    placed = (P(None, None, CHAN, TM), P(None, None, None, CHAN, TM), P(CHAN))
    return jax.shard_map(
        on_device,
        mesh=fine,
        in_specs=placed,
        out_specs=(P(None, None, CHAN, TM), P(None, None, CHAN, TM)),
        check_vma=False,
    )
```

```python
import jax
import jax.numpy as jnp
from jax import lax
from jax.experimental import pallas as pl
from jax.experimental.pallas import tpu as pltpu
from jax.sharding import Mesh, PartitionSpec as P

OPTICAL_CHANNELS = 64
FILTER_HALF_TAPS = 128
STEPS = 2
FIBER_SECTIONS = 1


ATT = 0.955
GAMMA = 0.004
WALK = 0.5
SPREAD = 0.4
CHIRP = 0.25
EPS = 1e-06


def tap_rows(channel_ids, sign, reach, channels):
    lag = jnp.arange(-reach, reach + 1, dtype=jnp.int32).astype(jnp.float32)[None, :]
    centre = WALK * reach * (2.0 * channel_ids.astype(jnp.float32) - (channels - 1)) / (channels - 1)
    centre = centre[:, None]
    width = SPREAD * reach
    offset = sign * lag - centre
    symbol_profile = jnp.exp(-jnp.square(offset / width))
    turn = jnp.square(offset) / (2.0 * CHIRP * reach)
    scale = jnp.sqrt(jnp.sum(jnp.exp(-2.0 * jnp.square((lag - centre) / width)), axis=1))[:, None]
    tap_re = symbol_profile * jnp.cos(turn) / scale
    tap_im = sign * symbol_profile * jnp.sin(turn) / scale
    return jnp.stack([tap_re, tap_im], axis=1)


def toeplitz_kernel(taps_ref, forward_ref, backward_ref):
    for slot in range(taps_ref.shape[0]):
        for sign, out_ref in enumerate((forward_ref, backward_ref)):
            toeplitz_fill(taps_ref.at[slot, sign], out_ref.at[slot])


def toeplitz_fill(taps_ref, out_ref):
    reach = out_ref.shape[-1] // 2
    for block in range(3):
        start = reach * (2 - block)
        parts = []
        for part in range(2):
            row = taps_ref[part : part + 1, start : start + 2 * reach]
            rolled = pltpu.roll(jnp.broadcast_to(row, (reach, 2 * reach)), 0, 1, stride=1, stride_axis=0)
            parts.append(rolled[:, reach:])
        real, imag = parts
        rows = slice(block * reach, (block + 1) * reach)
        out_ref[rows, :reach] = real
        out_ref[rows, reach:] = imag


def merged_tables(channel_ids, reach, channels):
    taps = jnp.stack([tap_rows(channel_ids, 1.0, reach, channels), tap_rows(channel_ids, -1.0, reach, channels)], axis=1)
    padded = jnp.pad(taps, ((0, 0), (0, 0), (0, 0), (reach, reach - 1)))
    count = taps.shape[0]
    table = jax.ShapeDtypeStruct((count, 3 * reach, 2 * reach), jnp.float32)
    per = 2
    block = pl.BlockSpec((per, 3 * reach, 2 * reach), lambda s: (s, 0, 0))
    return pl.pallas_call(
        toeplitz_kernel,
        grid=(count // per,),
        in_specs=[pl.BlockSpec((per, 2, 2, 4 * reach), lambda s: (s, 0, 0, 0))],
        out_specs=(block, block),
        out_shape=(table, table),
    )(padded)


def disperse(ext, table, reach):
    pols, parts, chans, segment_length = ext.shape
    blocks = segment_length // reach - 2
    rows = ext.reshape(pols, parts, chans, blocks + 2, reach)
    stacked = jnp.concatenate([rows[:, :, :, shift : shift + blocks] for shift in range(3)], axis=4)
    out = jnp.einsum("pacjq,cqn->pacjn", stacked, table, precision=lax.Precision.HIGHEST)
    from_re, from_im = out[:, 0], out[:, 1]
    real = from_re[..., :reach] - from_im[..., reach:]
    imag = from_re[..., reach:] + from_im[..., :reach]
    return jnp.stack([real, imag], axis=1).reshape(pols, parts, chans, blocks * reach)


def rotate(ext, sign, own, total):
    angle = sign * GAMMA * (2.0 * total[None, :] - own)
    cosine = jnp.cos(angle)
    sine = jnp.sin(angle)
    real = ext[:, 0]
    imag = ext[:, 1]
    return jnp.stack([real * cosine - imag * sine, real * sine + imag * cosine], axis=1)


TM = ("z", "xh", "xl", "yh")
CHAN = ("ylo", "core")


def psum_tm(value):
    for axis in ("yh", "xl", "xh", "z"):
        value = lax.psum(value, axis)
    return value


def psum_chan(value):
    for axis in ("core", "ylo"):
        value = lax.psum(value, axis)
    return value


def on_device(field, noise, assign):
    forward, backward = merged_tables(assign, FILTER_HALF_TAPS, OPTICAL_CHANNELS)
    total_len = lax.axis_size(TM) * field.shape[3]
    reach = FILTER_HALF_TAPS
    field_width = 2 * STEPS * reach
    noise_width = STEPS * reach

    def nonlinear(ext, sign):
        own = jnp.sum(jnp.square(ext), axis=(0, 1))
        total = psum_chan(jnp.sum(own, axis=0))
        return rotate(ext, sign, own, total)

    last_noise = noise[FIBER_SECTIONS - 1]
    count, length = lax.axis_size(TM), field.shape[3]
    up = [(i, (i + 1) % count) for i in range(count)]
    down = [(j, i) for i, j in up]
    halo_noise = last_noise
    last_noise = lax.optimization_barrier(last_noise)
    trailing = jnp.concatenate(
        [field[..., length - field_width :], halo_noise[..., length - noise_width :]], axis=3
    )
    leading = jnp.concatenate([field[..., :field_width], halo_noise[..., :noise_width]], axis=3)
    before = lax.ppermute(trailing, TM, up)
    after = lax.ppermute(leading, TM, down)
    current = jnp.concatenate([before[..., :field_width], field, after[..., :field_width]], axis=3)
    noise_ext = jnp.concatenate([before[..., field_width:], last_noise, after[..., field_width:]], axis=3)

    for step in range(STEPS):
        current = disperse(current, forward, reach) * ATT
        current = nonlinear(current, 1.0)
    centre = slice(noise_width, noise_width + length)
    signal, added = current[..., centre], last_noise
    sums = psum_tm(
        jnp.stack(
            [
                jnp.sum(jnp.square(signal), axis=(0, 1, 3)),
                jnp.sum(signal * added, axis=(0, 1, 3)),
                jnp.sum(jnp.square(added), axis=(0, 1, 3)),
            ]
        )
    )
    gain = lax.rsqrt(sums[0] / total_len + EPS)
    arrival = (gain * gain * sums[0] + 2.0 * gain * sums[1] + sums[2]) / total_len
    received = signal * gain[None, None, :, None] + added
    current = current * gain[None, None, :, None] + noise_ext
    rescale = jnp.sqrt(ATT ** (2 * STEPS) / (arrival + EPS))
    current = current * rescale[None, None, :, None]
    for step in range(STEPS):
        current = nonlinear(current, -1.0) / ATT
        current = disperse(current, backward, reach)
    return (received, current)


def solution(mesh):
    tm, chan = mesh.shape["tm"], mesh.shape["chan"]
    fine = Mesh(mesh.devices.reshape(tm // 16, 2, 4, 2, chan // 2, 2), TM + CHAN)
    placed = (P(None, None, CHAN, TM), P(None, None, None, CHAN, TM), P(CHAN))
    return jax.shard_map(
        on_device,
        mesh=fine,
        in_specs=placed,
        out_specs=(P(None, None, CHAN, TM), P(None, None, CHAN, TM)),
        check_vma=False,
    )
```
